256 devices in a mesh: sn: 64 (over y, z, core), rhs: 4 (over x).
Axes of the slice: x: 4, y: 4, z: 8, core: 2. Of those that a mesh axis runs over, the one named last changes fastest.
Arguments:
- leaf_rhs: float32 [256, 1024, 256], P('rhs', 'sn'), may hold values from -6 to 6
- root_rhs: float32 [256, 4096], P('rhs', 'sn'), may hold values from -6 to 6
- leaf_inverse: float32 [1024, 256, 256], P('sn'), as said below
- leaf_offdiagonal_block: float32 [1024, 128, 256], P('sn'), may hold values from -0.125 to 0.125
- update_rows: int32 [1024, 128], P('sn'), may hold values from 0 to 4095, as said below
- leaf_sizes: int32 [1024], P('sn'), may hold values from 1 to 256, 163840 in all
- root_inverse: float32 [4096, 4096], P('sn', 'rhs'), as said below
Outputs:
- leaf_solution: float32 [256, 1024, 256], P('rhs', 'sn')
- root_solution: float32 [256, 4096], P('rhs', 'sn')
The draws below stay inside these ranges and needn't reach their ends.
Inputs may be any that keep to these rules, and one draw needn't show every extreme that they name: `update_rows`: the 128 rows of one leaf are distinct. `leaf_inverse`: lower triangular with a positive diagonal. `root_inverse`: lower triangular with a positive diagonal.
All inputs are finite; a program needn't handle non-finite values. No bound on the sum of `leaf_sizes` on one device may be relied on, other than what follows from the above.
Results may differ from the reference program's by a relative error of at most 0.00015.
Values sent between devices are 32-bit elements; how exact they have to be, the bound alone decides.
No kernel may reach another device: no remote copies, remote signals or barrier semaphores. Data moves between devices by JAX's collectives and lax.ppermute only.
A program may use at most 64 MiB of HBM per device.

```python
import math
import jax
import jax.numpy as jnp
import numpy as np
from jax import lax

NRHS = 256
S = 256
K = 128
LEAVES = 1024
R = 4096


def triangle(key, shape, order):
    first_key, second_key = jax.random.split(key)
    row_index = lax.broadcasted_iota(jnp.int32, (order, order), 0)
    col_index = lax.broadcasted_iota(jnp.int32, (order, order), 1)
    below_mask = (col_index < row_index).astype(jnp.float32)
    diag_mask = (col_index == row_index).astype(jnp.float32)
    off_diag = jax.random.normal(first_key, shape, jnp.float32) * (0.5 / math.sqrt(order))
    diagonal_entries = jax.random.uniform(second_key, shape, jnp.float32, 0.75, 1.5)
    return off_diag * below_mask + diagonal_entries * diag_mask


def draw_leaf_inverse(key, part):
    return triangle(jax.random.fold_in(key, 11), (LEAVES, S, S), S)


def draw_root_inverse(key, part):
    return triangle(jax.random.fold_in(key, 23), (R, R), R)


def draw_update_rows(key, part):
    leaf_keys = jax.random.split(jax.random.fold_in(key, 37), LEAVES)
    return jax.vmap(lambda one_key: jax.random.permutation(one_key, R)[:K])(leaf_keys).astype(jnp.int32)


def block_scale(own_key, extent, pieces, low, largest):
    def one(dim, blocks):
        steps = jax.random.uniform(jax.random.fold_in(jax.random.fold_in(own_key, 6), dim), (blocks,), jnp.float32, low / len(pieces), largest / len(pieces))
        return jnp.repeat(jnp.exp(steps), extent[dim] // blocks).reshape((-1,) + (1,) * (len(extent) - dim - 1))

    gain = one(*pieces[0])
    for cut in pieces[1:]:
        gain = gain * one(*cut)
    return gain


def split_up(number_of, total, most, slope):
    portions = [(1 << 20) // math.isqrt(rank ** slope) + 1 for rank in range(2, number_of + 1)]
    surplus, counts = total - most - (number_of - 1), [1] * (number_of - 1)
    while surplus > 0:
        free = [i for i in range(number_of - 1) if counts[i] < most]
        mass, left = sum([portions[i] for i in free]), surplus
        for i in free:
            extra = min(most - counts[i], max(1, left * portions[i] // mass), surplus)
            counts[i] = counts[i] + extra
            surplus = surplus - extra
    return np.array([most] + counts)


def uneven_parts(rng, number_of, total, bound, slope):
    if number_of == 2:
        one = jax.random.randint(rng, (), max(1, total - bound), min(bound, total - 1) + 1)
        return jnp.stack([one, total - one])
    sizes = jnp.asarray(split_up(number_of, total, bound, slope), jnp.int32)
    couples = (number_of - 1) // 2
    giver, taker = sizes[1:1 + 2 * couples:2], sizes[2:2 + 2 * couples:2]
    room = jnp.minimum(giver - 1, bound - taker)
    passed = jax.random.randint(jax.random.fold_in(rng, 1), (couples,), 0, 1 << 20) % (room + 1)
    sizes = sizes.at[1:1 + 2 * couples:2].set(giver - passed).at[2:2 + 2 * couples:2].set(taker + passed)
    return sizes[jax.random.permutation(jax.random.fold_in(rng, 2), number_of)]


def gaussian(key, extent, spread, bound, cuts=(), kind=jnp.bfloat16):
    array = jax.random.normal(key, extent, jnp.float32) * spread
    if len(cuts) > 0:
        array = block_scale(key, extent, cuts, -0.22, 0.18) * array
    return jnp.clip(array, min=-bound, max=bound).astype(kind)


def setup_inputs(seed: int = 0) -> dict:
    key_list = jax.random.split(jax.random.key(seed), 8)
    leaf_rhs = gaussian(key_list[0], (NRHS, LEAVES, S), 1.0, 6.0, ((0, 4), (1, 64)), jnp.float32)
    root_rhs = gaussian(key_list[1], (NRHS, R), 1.0, 6.0, ((0, 4), (1, 64)), jnp.float32)
    leaf_inverse = draw_leaf_inverse(jax.random.fold_in(key_list[7], 71), 0)
    leaf_offdiagonal_block = gaussian(key_list[3], (LEAVES, K, S), (S * 8) ** -0.5, 0.125, ((0, 64),), jnp.float32)
    update_rows = draw_update_rows(jax.random.fold_in(key_list[7], 71), 0)
    leaf_sizes = uneven_parts(key_list[5], LEAVES, LEAVES * S * 5 // 8, S, 2).astype(jnp.int32)
    root_inverse = draw_root_inverse(jax.random.fold_in(key_list[7], 71), 0)
    return dict(leaf_rhs=leaf_rhs, root_rhs=root_rhs, leaf_inverse=leaf_inverse, leaf_offdiagonal_block=leaf_offdiagonal_block, update_rows=update_rows, leaf_sizes=leaf_sizes, root_inverse=root_inverse)


def reference(leaf_rhs, root_rhs, leaf_inverse, leaf_offdiagonal_block, update_rows, leaf_sizes, root_inverse):
    largest_entry = lax.Precision.HIGHEST
    slot_index = lax.broadcasted_iota(jnp.int32, (LEAVES, S), 1)
    live_mask = (slot_index < leaf_sizes[:, None]).astype(jnp.float32)
    masked = leaf_inverse * live_mask[:, :, None] * live_mask[:, None, :]
    leaf_forward_sweep = jnp.einsum("clt,lst->cls", leaf_rhs, masked, precision=largest_entry)
    update_terms = jnp.einsum("dwu,wqu->dwq", leaf_forward_sweep, leaf_offdiagonal_block, precision=largest_entry)
    flat_rows = update_rows.reshape(-1).astype(jnp.int32)
    accumulated_sum = jnp.zeros((NRHS, R), jnp.float32).at[:, flat_rows].add(update_terms.reshape(NRHS, LEAVES * K))
    reduced = root_rhs - accumulated_sum
    forward_root = jnp.einsum("cj,ij->ci", reduced, root_inverse, precision=largest_entry)
    root_solution = jnp.einsum("ci,ij->cj", forward_root, root_inverse, precision=largest_entry)
    selected_rows = jnp.take(root_solution, flat_rows, axis=1).reshape(NRHS, LEAVES, K)
    adjusted_values = leaf_forward_sweep - jnp.einsum("rnv,nvb->rnb", selected_rows, leaf_offdiagonal_block, precision=largest_entry)
    leaf_solution = jnp.einsum("cls,lst->clt", adjusted_values, masked, precision=largest_entry)
    return leaf_solution, root_solution
```

```python
import jax
import jax.numpy as jnp
from jax import lax
from jax.sharding import Mesh
from jax.sharding import PartitionSpec as P

LEAF_AXES = ("y", "z", "core")


def owner_sum(parts):
    core = lax.axis_index("core")
    columns, blocks, width = parts.shape
    pairs = parts.reshape(columns, blocks // 2, 2, width)
    mine = jnp.where(core == 1, pairs[:, :, 1], pairs[:, :, 0])
    other = jnp.where(core == 1, pairs[:, :, 0], pairs[:, :, 1])
    paired = mine + lax.ppermute(other, "core", [(0, 1), (1, 0)])
    spread = lax.all_to_all(paired.transpose(1, 0, 2), ("y", "z"), 0, 0, tiled=False)
    return spread.sum(0)


def share_all(block, blocks):
    columns, width = block.shape
    copies = jnp.broadcast_to(block[None], (blocks, columns, width))
    gathered = lax.all_to_all(copies, LEAF_AXES, 0, 0, tiled=False)
    return gathered.transpose(1, 0, 2).reshape(columns, blocks * width)


def on_device(
    leaf_rhs, root_rhs, leaf_inverse, leaf_offdiagonal_block, update_rows, leaf_sizes, root_inverse
):
    largest_entry = lax.Precision.HIGHEST
    leaf_count = leaf_inverse.shape[0]
    leaf_width = leaf_inverse.shape[1]
    touched = leaf_offdiagonal_block.shape[1]
    columns = leaf_rhs.shape[0]
    slot_index = lax.broadcasted_iota(jnp.int32, (leaf_count, leaf_width), 1)
    live_mask = (slot_index < leaf_sizes[:, None]).astype(jnp.float32)
    masked = leaf_inverse * live_mask[:, :, None] * live_mask[:, None, :]
    leaf_forward_sweep = jnp.einsum("clt,lst->cls", leaf_rhs, masked, precision=largest_entry)
    update_terms = jnp.einsum(
        "dwu,wqu->dwq", leaf_forward_sweep, leaf_offdiagonal_block, precision=largest_entry
    )
    root_full = lax.all_gather(root_inverse, "rhs", axis=1, tiled=True)
    root_order = root_full.shape[1]
    blocks = root_order // root_rhs.shape[1]
    flat_rows = update_rows.reshape(-1)
    accumulated_sum = (
        jnp.zeros((columns, root_order), jnp.float32)
        .at[:, flat_rows]
        .add(update_terms.reshape(columns, leaf_count * touched))
    )
    shares = owner_sum(accumulated_sum.reshape(columns, blocks, -1))
    reduced = root_rhs - shares
    forward_root = jnp.einsum(
        "cj,ij->ci",
        share_all(reduced, blocks),
        root_full,
        precision=largest_entry,
    )
    back_terms = jnp.einsum("ci,ij->cj", forward_root, root_full, precision=largest_entry)
    root_solution = owner_sum(back_terms.reshape(columns, blocks, -1))
    root_values = share_all(root_solution, blocks)
    selected_rows = jnp.take(root_values, flat_rows, axis=1).reshape(columns, leaf_count, touched)
    adjusted_values = leaf_forward_sweep - jnp.einsum(
        "rnv,nvb->rnb", selected_rows, leaf_offdiagonal_block, precision=largest_entry
    )
    leaf_solution = jnp.einsum("cls,lst->clt", adjusted_values, masked, precision=largest_entry)
    return (leaf_solution, root_solution)


def solution(mesh):
    sn_size = mesh.shape["sn"]
    fine = Mesh(
        mesh.devices.reshape(sn_size // 16, 8, 2, mesh.shape["rhs"]), ("y", "z", "core", "rhs")
    )
    sn = LEAF_AXES
    in_specs = (
        P("rhs", sn, None),
        P("rhs", sn),
        P(sn, None, None),
        P(sn, None, None),
        P(sn, None),
        P(sn),
        P(sn, "rhs"),
    )
    out_specs = (P("rhs", sn, None), P("rhs", sn))
    return jax.shard_map(
        on_device, mesh=fine, in_specs=in_specs, out_specs=out_specs, check_vma=False
    )
```

```python
import jax
import jax.numpy as jnp
from jax import lax
from jax.sharding import Mesh
from jax.sharding import PartitionSpec as P

LEAF_AXES = ("y", "z", "core")


def owner_sum(parts):
    core = lax.axis_index("core")
    blocks = parts.shape[0]
    pairs = parts.reshape(blocks // 2, 2, *parts.shape[1:])
    mine = jnp.where(core == 1, pairs[:, 1], pairs[:, 0])
    other = jnp.where(core == 1, pairs[:, 0], pairs[:, 1])
    paired = mine + lax.ppermute(other, "core", [(0, 1), (1, 0)])
    spread = lax.all_to_all(paired, ("y", "z"), 0, 0, tiled=False)
    return spread.sum(0)


def share_all(block, blocks):
    width, columns = block.shape
    copies = jnp.broadcast_to(block[None], (blocks, width, columns))
    gathered = lax.all_to_all(copies, LEAF_AXES, 0, 0, tiled=False)
    return gathered.reshape(blocks * width, columns)


def on_device(
    leaf_rhs, root_rhs, leaf_inverse, leaf_offdiagonal_block, update_rows, leaf_sizes, root_inverse
):
    largest_entry = lax.Precision.HIGHEST
    leaf_count = leaf_inverse.shape[0]
    leaf_width = leaf_inverse.shape[1]
    touched = leaf_offdiagonal_block.shape[1]
    columns = leaf_rhs.shape[0]
    slot_index = lax.broadcasted_iota(jnp.int32, (leaf_count, leaf_width), 1)
    live_mask = (slot_index < leaf_sizes[:, None]).astype(jnp.float32)
    masked = leaf_inverse * live_mask[:, :, None] * live_mask[:, None, :]
    leaf_forward_sweep = jnp.einsum("clt,lst->cls", leaf_rhs, masked, precision=largest_entry)
    update_terms = jnp.einsum(
        "dwu,wqu->wqd", leaf_forward_sweep, leaf_offdiagonal_block, precision=largest_entry
    )
    root_full = lax.all_gather(root_inverse, "rhs", axis=1, tiled=True)
    root_order = root_full.shape[1]
    width = root_rhs.shape[1]
    blocks = root_order // width
    flat_rows = update_rows.reshape(-1)
    accumulated_sum = (
        jnp.zeros((root_order, columns), jnp.float32)
        .at[flat_rows]
        .add(update_terms.reshape(leaf_count * touched, columns))
    )
    shares = owner_sum(accumulated_sum.reshape(blocks, width, columns))
    reduced = root_rhs.T - shares
    forward_root = jnp.einsum(
        "jc,ij->ic",
        share_all(reduced, blocks),
        root_full,
        precision=largest_entry,
    )
    back_terms = jnp.einsum("ic,ij->jc", forward_root, root_full, precision=largest_entry)
    root_solution = owner_sum(back_terms.reshape(blocks, width, columns))
    root_values = share_all(root_solution, blocks)
    selected_rows = jnp.take(root_values, flat_rows, axis=0).reshape(leaf_count, touched, columns)
    adjusted_values = leaf_forward_sweep - jnp.einsum(
        "nvr,nvb->rnb", selected_rows, leaf_offdiagonal_block, precision=largest_entry
    )
    leaf_solution = jnp.einsum("cls,lst->clt", adjusted_values, masked, precision=largest_entry)
    return (leaf_solution, root_solution.T)


def solution(mesh):
    sn_size = mesh.shape["sn"]
    fine = Mesh(
        mesh.devices.reshape(sn_size // 16, 8, 2, mesh.shape["rhs"]), ("y", "z", "core", "rhs")
    )
    sn = LEAF_AXES
    in_specs = (
        P("rhs", sn, None),
        P("rhs", sn),
        P(sn, None, None),
        P(sn, None, None),
        P(sn, None),
        P(sn),
        P(sn, "rhs"),
    )
    out_specs = (P("rhs", sn, None), P("rhs", sn))
    return jax.shard_map(
        on_device, mesh=fine, in_specs=in_specs, out_specs=out_specs, check_vma=False
    )
```

```python
import jax
import jax.numpy as jnp
from jax import lax
from jax.sharding import Mesh
from jax.sharding import PartitionSpec as P

LEAF_AXES = ("y", "z", "core")


def owner_sum(parts):
    core = lax.axis_index("core")
    blocks = parts.shape[0]
    pairs = parts.reshape(blocks // 2, 2, *parts.shape[1:])
    mine = jnp.where(core == 1, pairs[:, 1], pairs[:, 0])
    other = jnp.where(core == 1, pairs[:, 0], pairs[:, 1])
    paired = mine + lax.ppermute(other, "core", [(0, 1), (1, 0)])
    spread = lax.all_to_all(paired, ("y", "z"), 0, 0, tiled=False)
    return spread.sum(0)


def share_all(block, blocks):
    width, columns = block.shape
    copies = jnp.broadcast_to(block[None], (blocks, width, columns))
    gathered = lax.all_to_all(copies, LEAF_AXES, 0, 0, tiled=False)
    return gathered.reshape(blocks * width, columns)


def on_device(
    leaf_rhs, root_rhs, leaf_inverse, leaf_offdiagonal_block, update_rows, leaf_sizes, root_inverse
):
    largest_entry = lax.Precision.HIGH
    leaf_count = leaf_inverse.shape[0]
    leaf_width = leaf_inverse.shape[1]
    touched = leaf_offdiagonal_block.shape[1]
    columns = leaf_rhs.shape[0]
    slot_index = lax.broadcasted_iota(jnp.int32, (leaf_count, leaf_width), 1)
    live_mask = (slot_index < leaf_sizes[:, None]).astype(jnp.float32)
    masked = leaf_inverse * live_mask[:, :, None] * live_mask[:, None, :]
    leaf_forward_sweep = jnp.einsum("clt,lst->cls", leaf_rhs, masked, precision=largest_entry)
    update_terms = jnp.einsum(
        "dwu,wqu->wqd", leaf_forward_sweep, leaf_offdiagonal_block, precision=largest_entry
    )
    swept_twice = jnp.einsum("cls,lst->clt", leaf_forward_sweep, masked, precision=largest_entry)
    block_sweep = jnp.einsum(
        "lks,lst->lkt", leaf_offdiagonal_block, masked, precision=largest_entry
    )
    root_full = lax.all_gather(root_inverse, "rhs", axis=1, tiled=True)
    root_order = root_full.shape[1]
    width = root_rhs.shape[1]
    blocks = root_order // width
    flat_rows = update_rows.reshape(-1)
    accumulated_sum = (
        jnp.zeros((root_order, columns), jnp.float32)
        .at[flat_rows]
        .add(update_terms.reshape(leaf_count * touched, columns))
    )
    shares = owner_sum(accumulated_sum.reshape(blocks, width, columns))
    reduced = root_rhs.T - shares
    forward_root = jnp.einsum(
        "jc,ij->ic",
        share_all(reduced, blocks),
        root_full,
        precision=largest_entry,
    )
    back_terms = jnp.einsum("ic,ij->jc", forward_root, root_full, precision=largest_entry)
    root_solution = owner_sum(back_terms.reshape(blocks, width, columns))
    root_values = share_all(root_solution, blocks)
    selected_rows = jnp.take(root_values, flat_rows, axis=0).reshape(leaf_count, touched, columns)
    leaf_solution = swept_twice - jnp.einsum(
        "nvr,nvb->rnb", selected_rows, block_sweep, precision=largest_entry
    )
    return (leaf_solution, root_solution.T)


def solution(mesh):
    sn_size = mesh.shape["sn"]
    fine = Mesh(
        mesh.devices.reshape(sn_size // 16, 8, 2, mesh.shape["rhs"]), ("y", "z", "core", "rhs")
    )
    sn = LEAF_AXES
    in_specs = (
        P("rhs", sn, None),
        P("rhs", sn),
        P(sn, None, None),
        P(sn, None, None),
        P(sn, None),
        P(sn),
        P(sn, "rhs"),
    )
    out_specs = (P("rhs", sn, None), P("rhs", sn))
    return jax.shard_map(
        on_device, mesh=fine, in_specs=in_specs, out_specs=out_specs, check_vma=False
    )
```

```python
import jax
import jax.numpy as jnp
from jax import lax
from jax.sharding import Mesh
from jax.sharding import PartitionSpec as P

LEAF_AXES = ("y", "z", "core")


def owner_sum(parts):
    core = lax.axis_index("core")
    blocks = parts.shape[0]
    pairs = parts.reshape(blocks // 2, 2, *parts.shape[1:])
    mine = jnp.where(core == 1, pairs[:, 1], pairs[:, 0])
    other = jnp.where(core == 1, pairs[:, 0], pairs[:, 1])
    paired = mine + lax.ppermute(other, "core", [(0, 1), (1, 0)])
    spread = lax.all_to_all(paired, ("y", "z"), 0, 0, tiled=False)
    return spread.sum(0)


def share_all(block, blocks):
    width, columns = block.shape
    copies = jnp.broadcast_to(block[None], (blocks, width, columns))
    gathered = lax.all_to_all(copies, LEAF_AXES, 0, 0, tiled=False)
    return gathered.reshape(blocks * width, columns)


def on_device(
    leaf_rhs, root_rhs, leaf_inverse, leaf_offdiagonal_block, update_rows, leaf_sizes, root_inverse
):
    largest_entry = lax.Precision.HIGH
    leaf_count = leaf_inverse.shape[0]
    leaf_width = leaf_inverse.shape[1]
    touched = leaf_offdiagonal_block.shape[1]
    columns = leaf_rhs.shape[0]
    slot_index = lax.broadcasted_iota(jnp.int32, (leaf_count, leaf_width), 1)
    live_mask = (slot_index < leaf_sizes[:, None]).astype(jnp.float32)
    masked = leaf_inverse * live_mask[:, :, None] * live_mask[:, None, :]
    leaf_forward_sweep = jnp.einsum("clt,lst->cls", leaf_rhs, masked, precision=largest_entry)
    update_terms = jnp.einsum(
        "dwu,wqu->wqd", leaf_forward_sweep, leaf_offdiagonal_block, precision=largest_entry
    )
    root_full = lax.all_gather(root_inverse, "rhs", axis=1, tiled=True)
    root_order = root_full.shape[1]
    width = root_rhs.shape[1]
    blocks = root_order // width
    flat_rows = update_rows.reshape(-1)
    accumulated_sum = (
        jnp.zeros((root_order, columns), jnp.float32)
        .at[flat_rows]
        .add(update_terms.reshape(leaf_count * touched, columns))
    )
    shares = owner_sum(accumulated_sum.reshape(blocks, width, columns))
    reduced = root_rhs.T - shares
    forward_root = jnp.einsum(
        "jc,ij->ic",
        share_all(reduced, blocks),
        root_full,
        precision=largest_entry,
    )
    back_terms = jnp.einsum("ic,ij->jc", forward_root, root_full, precision=largest_entry)
    root_solution = owner_sum(back_terms.reshape(blocks, width, columns))
    root_values = share_all(root_solution, blocks)
    selected_rows = jnp.take(root_values, flat_rows, axis=0).reshape(leaf_count, touched, columns)
    adjusted_values = leaf_forward_sweep - jnp.einsum(
        "nvr,nvb->rnb", selected_rows, leaf_offdiagonal_block, precision=largest_entry
    )
    leaf_solution = jnp.einsum("cls,lst->clt", adjusted_values, masked, precision=largest_entry)
    return (leaf_solution, root_solution.T)


def solution(mesh):
    sn_size = mesh.shape["sn"]
    fine = Mesh(
        mesh.devices.reshape(sn_size // 16, 8, 2, mesh.shape["rhs"]), ("y", "z", "core", "rhs")
    )
    sn = LEAF_AXES
    in_specs = (
        P("rhs", sn, None),
        P("rhs", sn),
        P(sn, None, None),
        P(sn, None, None),
        P(sn, None),
        P(sn),
        P(sn, "rhs"),
    )
    out_specs = (P("rhs", sn, None), P("rhs", sn))
    return jax.shard_map(
        on_device, mesh=fine, in_specs=in_specs, out_specs=out_specs, check_vma=False
    )
```

```python
import jax
import jax.numpy as jnp
from jax import lax
from jax.sharding import Mesh
from jax.sharding import PartitionSpec as P

LEAF_AXES = ("y", "z", "core")


def owner_sum(parts):
    core = lax.axis_index("core")
    blocks, width, columns = parts.shape
    pairs = parts.reshape(blocks // 2, 2, 8, width * columns // 8)
    mine = jnp.where(core == 1, pairs[:, 1], pairs[:, 0])
    other = jnp.where(core == 1, pairs[:, 0], pairs[:, 1])
    paired = mine + lax.ppermute(other, "core", [(0, 1), (1, 0)])
    spread = lax.all_to_all(paired, ("y", "z"), 0, 0, tiled=False)
    return spread.sum(0).reshape(width, columns)


def share_all(block, blocks):
    width, columns = block.shape
    flat = block.reshape(1, 8, width * columns // 8)
    copies = jnp.broadcast_to(flat, (blocks, 8, width * columns // 8))
    gathered = lax.all_to_all(copies, LEAF_AXES, 0, 0, tiled=False)
    return gathered.reshape(blocks * width, columns)


def on_device(
    leaf_rhs, root_rhs, leaf_inverse, leaf_offdiagonal_block, update_rows, leaf_sizes, root_inverse
):
    largest_entry = lax.Precision.HIGH
    leaf_count = leaf_inverse.shape[0]
    leaf_width = leaf_inverse.shape[1]
    touched = leaf_offdiagonal_block.shape[1]
    columns = leaf_rhs.shape[0]
    slot_index = lax.broadcasted_iota(jnp.int32, (leaf_count, leaf_width), 1)
    live_mask = (slot_index < leaf_sizes[:, None]).astype(jnp.float32)
    masked = leaf_inverse * live_mask[:, :, None] * live_mask[:, None, :]
    leaf_forward_sweep = jnp.einsum("clt,lst->cls", leaf_rhs, masked, precision=largest_entry)
    update_terms = jnp.einsum(
        "dwu,wqu->wqd", leaf_forward_sweep, leaf_offdiagonal_block, precision=largest_entry
    )
    root_full = lax.all_gather(root_inverse, "rhs", axis=1, tiled=True)
    root_order = root_full.shape[1]
    width = root_rhs.shape[1]
    blocks = root_order // width
    flat_rows = update_rows.reshape(-1)
    accumulated_sum = (
        jnp.zeros((root_order, columns), jnp.float32)
        .at[flat_rows]
        .add(update_terms.reshape(leaf_count * touched, columns))
    )
    shares = owner_sum(accumulated_sum.reshape(blocks, width, columns))
    reduced = root_rhs.T - shares
    forward_root = jnp.einsum(
        "jc,ij->ic",
        share_all(reduced, blocks),
        root_full,
        precision=largest_entry,
    )
    back_terms = jnp.einsum("ic,ij->jc", forward_root, root_full, precision=largest_entry)
    root_solution = owner_sum(back_terms.reshape(blocks, width, columns))
    root_values = share_all(root_solution, blocks)
    selected_rows = jnp.take(root_values, flat_rows, axis=0).reshape(leaf_count, touched, columns)
    adjusted_values = leaf_forward_sweep - jnp.einsum(
        "nvr,nvb->rnb", selected_rows, leaf_offdiagonal_block, precision=largest_entry
    )
    leaf_solution = jnp.einsum("cls,lst->clt", adjusted_values, masked, precision=largest_entry)
    return (leaf_solution, root_solution.T)


def solution(mesh):
    sn_size = mesh.shape["sn"]
    fine = Mesh(
        mesh.devices.reshape(sn_size // 16, 8, 2, mesh.shape["rhs"]), ("y", "z", "core", "rhs")
    )
    sn = LEAF_AXES
    in_specs = (
        P("rhs", sn, None),
        P("rhs", sn),
        P(sn, None, None),
        P(sn, None, None),
        P(sn, None),
        P(sn),
        P(sn, "rhs"),
    )
    out_specs = (P("rhs", sn, None), P("rhs", sn))
    return jax.shard_map(
        on_device, mesh=fine, in_specs=in_specs, out_specs=out_specs, check_vma=False
    )
```

```python
import jax
import jax.numpy as jnp
from jax import lax
from jax.sharding import Mesh
from jax.sharding import PartitionSpec as P

LEAF_AXES = ("y", "z", "core")


def owner_sum(parts):
    core = lax.axis_index("core")
    blocks, width, columns = parts.shape
    pairs = parts.reshape(blocks // 2, 2, 8, width * columns // 8)
    mine = jnp.where(core == 1, pairs[:, 1], pairs[:, 0])
    other = jnp.where(core == 1, pairs[:, 0], pairs[:, 1])
    paired = mine + lax.ppermute(other, "core", [(0, 1), (1, 0)])
    spread = lax.all_to_all(paired, ("y", "z"), 0, 0, tiled=False)
    return spread.sum(0).reshape(width, columns)


def share_all(block, blocks):
    width, columns = block.shape
    core = lax.axis_index("core")
    flat = block.reshape(8, width * columns // 8)
    partner = lax.ppermute(flat, "core", [(0, 1), (1, 0)])
    pair = jnp.where(core == 1, jnp.stack([partner, flat]), jnp.stack([flat, partner]))
    copies = jnp.broadcast_to(pair[None], (blocks // 2, *pair.shape))
    gathered = lax.all_to_all(copies, ("y", "z"), 0, 0, tiled=False)
    return gathered.reshape(blocks * width, columns)


def on_device(
    leaf_rhs, root_rhs, leaf_inverse, leaf_offdiagonal_block, update_rows, leaf_sizes, root_inverse
):
    largest_entry = lax.Precision.HIGH
    leaf_count = leaf_inverse.shape[0]
    leaf_width = leaf_inverse.shape[1]
    touched = leaf_offdiagonal_block.shape[1]
    columns = leaf_rhs.shape[0]
    slot_index = lax.broadcasted_iota(jnp.int32, (leaf_count, leaf_width), 1)
    live_mask = (slot_index < leaf_sizes[:, None]).astype(jnp.float32)
    masked = leaf_inverse * live_mask[:, :, None] * live_mask[:, None, :]
    leaf_forward_sweep = jnp.einsum("clt,lst->cls", leaf_rhs, masked, precision=largest_entry)
    update_terms = jnp.einsum(
        "dwu,wqu->wqd", leaf_forward_sweep, leaf_offdiagonal_block, precision=largest_entry
    )
    root_full = lax.all_gather(root_inverse, "rhs", axis=1, tiled=True)
    root_order = root_full.shape[1]
    width = root_rhs.shape[1]
    blocks = root_order // width
    flat_rows = update_rows.reshape(-1)
    accumulated_sum = (
        jnp.zeros((root_order, columns), jnp.float32)
        .at[flat_rows]
        .add(update_terms.reshape(leaf_count * touched, columns))
    )
    shares = owner_sum(accumulated_sum.reshape(blocks, width, columns))
    reduced = root_rhs.T - shares
    forward_root = jnp.einsum(
        "jc,ij->ic",
        share_all(reduced, blocks),
        root_full,
        precision=largest_entry,
    )
    back_terms = jnp.einsum("ic,ij->jc", forward_root, root_full, precision=largest_entry)
    root_solution = owner_sum(back_terms.reshape(blocks, width, columns))
    root_values = share_all(root_solution, blocks)
    selected_rows = jnp.take(root_values, flat_rows, axis=0).reshape(leaf_count, touched, columns)
    adjusted_values = leaf_forward_sweep - jnp.einsum(
        "nvr,nvb->rnb", selected_rows, leaf_offdiagonal_block, precision=largest_entry
    )
    leaf_solution = jnp.einsum("cls,lst->clt", adjusted_values, masked, precision=largest_entry)
    return (leaf_solution, root_solution.T)


def solution(mesh):
    sn_size = mesh.shape["sn"]
    fine = Mesh(
        mesh.devices.reshape(sn_size // 16, 8, 2, mesh.shape["rhs"]), ("y", "z", "core", "rhs")
    )
    sn = LEAF_AXES
    in_specs = (
        P("rhs", sn, None),
        P("rhs", sn),
        P(sn, None, None),
        P(sn, None, None),
        P(sn, None),
        P(sn),
        P(sn, "rhs"),
    )
    out_specs = (P("rhs", sn, None), P("rhs", sn))
    return jax.shard_map(
        on_device, mesh=fine, in_specs=in_specs, out_specs=out_specs, check_vma=False
    )
```

```python
import jax
import jax.numpy as jnp
from jax import lax
from jax.sharding import Mesh
from jax.sharding import PartitionSpec as P

LEAF_AXES = ("y", "z", "core")


def owner_sum(parts):
    core = lax.axis_index("core")
    blocks, width, columns = parts.shape
    pairs = parts.reshape(blocks // 2, 2, 8, width * columns // 8)
    mine = jnp.where(core == 1, pairs[:, 1], pairs[:, 0])
    other = jnp.where(core == 1, pairs[:, 0], pairs[:, 1])
    paired = mine + lax.ppermute(other, "core", [(0, 1), (1, 0)])
    spread = lax.all_to_all(paired, ("y", "z"), 0, 0, tiled=False)
    return spread.sum(0).reshape(width, columns)


def share_all(block, blocks):
    width, columns = block.shape
    flat = block.reshape(1, 8, width * columns // 8)
    copies = jnp.broadcast_to(flat, (blocks, 8, width * columns // 8))
    gathered = lax.all_to_all(copies, LEAF_AXES, 0, 0, tiled=False)
    return gathered.reshape(blocks * width, columns)


def gather_columns(part):
    count = lax.axis_size("rhs")
    place = lax.axis_index("rhs")
    shifted = [part] + [
        lax.ppermute(part, "rhs", [(i, (i + step) % count) for i in range(count)])
        for step in range(1, count)
    ]
    ahead = jnp.stack([shifted[(count - t) % count] for t in range(count)])
    ordered = jnp.roll(ahead, place, axis=0)
    rows, width = part.shape
    return ordered.transpose(1, 0, 2).reshape(rows, count * width)


def on_device(
    leaf_rhs, root_rhs, leaf_inverse, leaf_offdiagonal_block, update_rows, leaf_sizes, root_inverse
):
    largest_entry = lax.Precision.HIGH
    leaf_count = leaf_inverse.shape[0]
    leaf_width = leaf_inverse.shape[1]
    touched = leaf_offdiagonal_block.shape[1]
    columns = leaf_rhs.shape[0]
    slot_index = lax.broadcasted_iota(jnp.int32, (leaf_count, leaf_width), 1)
    live_mask = (slot_index < leaf_sizes[:, None]).astype(jnp.float32)
    masked = leaf_inverse * live_mask[:, :, None] * live_mask[:, None, :]
    leaf_forward_sweep = jnp.einsum("clt,lst->cls", leaf_rhs, masked, precision=largest_entry)
    update_terms = jnp.einsum(
        "dwu,wqu->wqd", leaf_forward_sweep, leaf_offdiagonal_block, precision=largest_entry
    )
    root_full = gather_columns(root_inverse)
    root_order = root_full.shape[1]
    width = root_rhs.shape[1]
    blocks = root_order // width
    flat_rows = update_rows.reshape(-1)
    accumulated_sum = (
        jnp.zeros((root_order, columns), jnp.float32)
        .at[flat_rows]
        .add(update_terms.reshape(leaf_count * touched, columns))
    )
    shares = owner_sum(accumulated_sum.reshape(blocks, width, columns))
    reduced = root_rhs.T - shares
    forward_root = jnp.einsum(
        "jc,ij->ic",
        share_all(reduced, blocks),
        root_full,
        precision=largest_entry,
    )
    back_terms = jnp.einsum("ic,ij->jc", forward_root, root_full, precision=largest_entry)
    root_solution = owner_sum(back_terms.reshape(blocks, width, columns))
    root_values = share_all(root_solution, blocks)
    selected_rows = jnp.take(root_values, flat_rows, axis=0).reshape(leaf_count, touched, columns)
    adjusted_values = leaf_forward_sweep - jnp.einsum(
        "nvr,nvb->rnb", selected_rows, leaf_offdiagonal_block, precision=largest_entry
    )
    leaf_solution = jnp.einsum("cls,lst->clt", adjusted_values, masked, precision=largest_entry)
    return (leaf_solution, root_solution.T)


def solution(mesh):
    sn_size = mesh.shape["sn"]
    fine = Mesh(
        mesh.devices.reshape(sn_size // 16, 8, 2, mesh.shape["rhs"]), ("y", "z", "core", "rhs")
    )
    sn = LEAF_AXES
    in_specs = (
        P("rhs", sn, None),
        P("rhs", sn),
        P(sn, None, None),
        P(sn, None, None),
        P(sn, None),
        P(sn),
        P(sn, "rhs"),
    )
    out_specs = (P("rhs", sn, None), P("rhs", sn))
    return jax.shard_map(
        on_device, mesh=fine, in_specs=in_specs, out_specs=out_specs, check_vma=False
    )
```

```python
import jax
import jax.numpy as jnp
from jax import lax
from jax.experimental import pallas as pl
from jax.experimental.pallas import tpu as pltpu
from jax.sharding import Mesh
from jax.sharding import PartitionSpec as P

LEAF_AXES = ("y", "z", "core")


GROUP = 8


def scatter_rows(rows, updates, order):
    count, columns = updates.shape

    def kernel(rows_ref, upd_ref, out_ref):
        out_ref[...] = jnp.zeros_like(out_ref)

        def body(group, carry):
            base = group * GROUP
            targets = [rows_ref[base + u] for u in range(GROUP)]
            sums = [
                out_ref[pl.ds(targets[u], 1), :] + upd_ref[pl.ds(base + u, 1), :]
                for u in range(GROUP)
            ]
            for u in range(GROUP):
                out_ref[pl.ds(targets[u], 1), :] = sums[u]
            return carry

        lax.fori_loop(0, count // GROUP, body, 0)

    return pl.pallas_call(
        kernel,
        out_shape=jax.ShapeDtypeStruct((order, columns), jnp.float32),
        grid_spec=pltpu.PrefetchScalarGridSpec(
            num_scalar_prefetch=1,
            grid=(1,),
            in_specs=[pl.BlockSpec((count, columns), lambda i, r: (0, 0))],
            out_specs=pl.BlockSpec((order, columns), lambda i, r: (0, 0)),
        ),
    )(rows, updates)


def owner_sum(parts):
    core = lax.axis_index("core")
    blocks, width, columns = parts.shape
    pairs = parts.reshape(blocks // 2, 2, 8, width * columns // 8)
    mine = jnp.where(core == 1, pairs[:, 1], pairs[:, 0])
    other = jnp.where(core == 1, pairs[:, 0], pairs[:, 1])
    paired = mine + lax.ppermute(other, "core", [(0, 1), (1, 0)])
    spread = lax.all_to_all(paired, ("y", "z"), 0, 0, tiled=False)
    return spread.sum(0).reshape(width, columns)


def share_all(block, blocks):
    width, columns = block.shape
    flat = block.reshape(1, 8, width * columns // 8)
    copies = jnp.broadcast_to(flat, (blocks, 8, width * columns // 8))
    gathered = lax.all_to_all(copies, LEAF_AXES, 0, 0, tiled=False)
    return gathered.reshape(blocks * width, columns)


def gather_columns(part):
    count = lax.axis_size("rhs")
    place = lax.axis_index("rhs")
    shifted = [part] + [
        lax.ppermute(part, "rhs", [(i, (i + step) % count) for i in range(count)])
        for step in range(1, count)
    ]
    ahead = jnp.stack([shifted[(count - t) % count] for t in range(count)])
    ordered = jnp.roll(ahead, place, axis=0)
    rows, width = part.shape
    return ordered.transpose(1, 0, 2).reshape(rows, count * width)


def on_device(
    leaf_rhs, root_rhs, leaf_inverse, leaf_offdiagonal_block, update_rows, leaf_sizes, root_inverse
):
    largest_entry = lax.Precision.HIGH
    leaf_count = leaf_inverse.shape[0]
    leaf_width = leaf_inverse.shape[1]
    touched = leaf_offdiagonal_block.shape[1]
    columns = leaf_rhs.shape[0]
    slot_index = lax.broadcasted_iota(jnp.int32, (leaf_count, leaf_width), 1)
    live_mask = (slot_index < leaf_sizes[:, None]).astype(jnp.float32)
    masked = leaf_inverse * live_mask[:, :, None] * live_mask[:, None, :]
    leaf_forward_sweep = jnp.einsum("clt,lst->cls", leaf_rhs, masked, precision=largest_entry)
    update_terms = jnp.einsum(
        "dwu,wqu->wqd", leaf_forward_sweep, leaf_offdiagonal_block, precision=largest_entry
    )
    root_full = gather_columns(root_inverse)
    root_order = root_full.shape[1]
    width = root_rhs.shape[1]
    blocks = root_order // width
    flat_rows = update_rows.reshape(-1)
    assert touched % GROUP == 0
    accumulated_sum = scatter_rows(
        flat_rows, update_terms.reshape(leaf_count * touched, columns), root_order
    )
    shares = owner_sum(accumulated_sum.reshape(blocks, width, columns))
    reduced = root_rhs.T - shares
    forward_root = jnp.einsum(
        "jc,ij->ic",
        share_all(reduced, blocks),
        root_full,
        precision=largest_entry,
    )
    back_terms = jnp.einsum("ic,ij->jc", forward_root, root_full, precision=largest_entry)
    root_solution = owner_sum(back_terms.reshape(blocks, width, columns))
    root_values = share_all(root_solution, blocks)
    selected_rows = jnp.take(root_values, flat_rows, axis=0).reshape(leaf_count, touched, columns)
    adjusted_values = leaf_forward_sweep - jnp.einsum(
        "nvr,nvb->rnb", selected_rows, leaf_offdiagonal_block, precision=largest_entry
    )
    leaf_solution = jnp.einsum("cls,lst->clt", adjusted_values, masked, precision=largest_entry)
    return (leaf_solution, root_solution.T)


def solution(mesh):
    sn_size = mesh.shape["sn"]
    fine = Mesh(
        mesh.devices.reshape(sn_size // 16, 8, 2, mesh.shape["rhs"]), ("y", "z", "core", "rhs")
    )
    sn = LEAF_AXES
    in_specs = (
        P("rhs", sn, None),
        P("rhs", sn),
        P(sn, None, None),
        P(sn, None, None),
        P(sn, None),
        P(sn),
        P(sn, "rhs"),
    )
    out_specs = (P("rhs", sn, None), P("rhs", sn))
    return jax.shard_map(
        on_device, mesh=fine, in_specs=in_specs, out_specs=out_specs, check_vma=False
    )
```

```python
import jax
import jax.numpy as jnp
from jax import lax
from jax.experimental import pallas as pl
from jax.experimental.pallas import tpu as pltpu
from jax.sharding import Mesh
from jax.sharding import PartitionSpec as P

LEAF_AXES = ("y", "z", "core")


GROUP = 16


def scatter_rows(rows, updates, order):
    count, columns = updates.shape

    def kernel(rows_ref, upd_ref, out_ref):
        out_ref[...] = jnp.zeros_like(out_ref)

        def body(group, carry):
            base = group * GROUP
            targets = [rows_ref[base + u] for u in range(GROUP)]
            sums = [
                out_ref[pl.ds(targets[u], 1), :] + upd_ref[pl.ds(base + u, 1), :]
                for u in range(GROUP)
            ]
            for u in range(GROUP):
                out_ref[pl.ds(targets[u], 1), :] = sums[u]
            return carry

        lax.fori_loop(0, count // GROUP, body, 0)

    return pl.pallas_call(
        kernel,
        out_shape=jax.ShapeDtypeStruct((order, columns), jnp.float32),
        grid_spec=pltpu.PrefetchScalarGridSpec(
            num_scalar_prefetch=1,
            grid=(1,),
            in_specs=[pl.BlockSpec((count, columns), lambda i, r: (0, 0))],
            out_specs=pl.BlockSpec((order, columns), lambda i, r: (0, 0)),
        ),
    )(rows, updates)


def gather_rows(rows, table):
    count = rows.shape[0]
    order, columns = table.shape

    def kernel(rows_ref, table_ref, out_ref):
        def body(group, carry):
            base = group * GROUP
            picked = [table_ref[pl.ds(rows_ref[base + u], 1), :] for u in range(GROUP)]
            for u in range(GROUP):
                out_ref[pl.ds(base + u, 1), :] = picked[u]
            return carry

        lax.fori_loop(0, count // GROUP, body, 0)

    return pl.pallas_call(
        kernel,
        out_shape=jax.ShapeDtypeStruct((count, columns), jnp.float32),
        grid_spec=pltpu.PrefetchScalarGridSpec(
            num_scalar_prefetch=1,
            grid=(1,),
            in_specs=[pl.BlockSpec((order, columns), lambda i, r: (0, 0))],
            out_specs=pl.BlockSpec((count, columns), lambda i, r: (0, 0)),
        ),
    )(rows, table)


def owner_sum(parts):
    core = lax.axis_index("core")
    blocks, width, columns = parts.shape
    pairs = parts.reshape(blocks // 2, 2, 8, width * columns // 8)
    mine = jnp.where(core == 1, pairs[:, 1], pairs[:, 0])
    other = jnp.where(core == 1, pairs[:, 0], pairs[:, 1])
    paired = mine + lax.ppermute(other, "core", [(0, 1), (1, 0)])
    spread = lax.all_to_all(paired, ("y", "z"), 0, 0, tiled=False)
    return spread.sum(0).reshape(width, columns)


def share_all(block, blocks):
    width, columns = block.shape
    flat = block.reshape(1, 8, width * columns // 8)
    copies = jnp.broadcast_to(flat, (blocks, 8, width * columns // 8))
    gathered = lax.all_to_all(copies, LEAF_AXES, 0, 0, tiled=False)
    return gathered.reshape(blocks * width, columns)


def gather_columns(part):
    count = lax.axis_size("rhs")
    place = lax.axis_index("rhs")
    shifted = [part] + [
        lax.ppermute(part, "rhs", [(i, (i + step) % count) for i in range(count)])
        for step in range(1, count)
    ]
    ahead = jnp.stack([shifted[(count - t) % count] for t in range(count)])
    ordered = jnp.roll(ahead, place, axis=0)
    rows, width = part.shape
    return ordered.transpose(1, 0, 2).reshape(rows, count * width)


def on_device(
    leaf_rhs, root_rhs, leaf_inverse, leaf_offdiagonal_block, update_rows, leaf_sizes, root_inverse
):
    largest_entry = lax.Precision.HIGH
    leaf_count = leaf_inverse.shape[0]
    leaf_width = leaf_inverse.shape[1]
    touched = leaf_offdiagonal_block.shape[1]
    columns = leaf_rhs.shape[0]
    slot_index = lax.broadcasted_iota(jnp.int32, (leaf_count, leaf_width), 1)
    live_mask = (slot_index < leaf_sizes[:, None]).astype(jnp.float32)
    masked = leaf_inverse * live_mask[:, :, None] * live_mask[:, None, :]
    leaf_forward_sweep = jnp.einsum("clt,lst->cls", leaf_rhs, masked, precision=largest_entry)
    update_terms = jnp.einsum(
        "dwu,wqu->wqd", leaf_forward_sweep, leaf_offdiagonal_block, precision=largest_entry
    )
    root_full = gather_columns(root_inverse)
    root_order = root_full.shape[1]
    width = root_rhs.shape[1]
    blocks = root_order // width
    flat_rows = update_rows.reshape(-1)
    assert touched % GROUP == 0
    accumulated_sum = scatter_rows(
        flat_rows, update_terms.reshape(leaf_count * touched, columns), root_order
    )
    shares = owner_sum(accumulated_sum.reshape(blocks, width, columns))
    reduced = root_rhs.T - shares
    forward_root = jnp.einsum(
        "jc,ij->ic",
        share_all(reduced, blocks),
        root_full,
        precision=largest_entry,
    )
    back_terms = jnp.einsum("ic,ij->jc", forward_root, root_full, precision=largest_entry)
    root_solution = owner_sum(back_terms.reshape(blocks, width, columns))
    root_values = share_all(root_solution, blocks)
    selected_rows = gather_rows(flat_rows, root_values).reshape(leaf_count, touched, columns)
    adjusted_values = leaf_forward_sweep - jnp.einsum(
        "nvr,nvb->rnb", selected_rows, leaf_offdiagonal_block, precision=largest_entry
    )
    leaf_solution = jnp.einsum("cls,lst->clt", adjusted_values, masked, precision=largest_entry)
    return (leaf_solution, root_solution.T)


def solution(mesh):
    sn_size = mesh.shape["sn"]
    fine = Mesh(
        mesh.devices.reshape(sn_size // 16, 8, 2, mesh.shape["rhs"]), ("y", "z", "core", "rhs")
    )
    sn = LEAF_AXES
    in_specs = (
        P("rhs", sn, None),
        P("rhs", sn),
        P(sn, None, None),
        P(sn, None, None),
        P(sn, None),
        P(sn),
        P(sn, "rhs"),
    )
    out_specs = (P("rhs", sn, None), P("rhs", sn))
    return jax.shard_map(
        on_device, mesh=fine, in_specs=in_specs, out_specs=out_specs, check_vma=False
    )
```

```python
import jax
import jax.numpy as jnp
from jax import lax
from jax.experimental import pallas as pl
from jax.experimental.pallas import tpu as pltpu
from jax.sharding import Mesh
from jax.sharding import PartitionSpec as P

LEAF_AXES = ("y", "z", "core")


GROUP = 32


def scatter_rows(rows, updates, order):
    count, columns = updates.shape

    def kernel(rows_ref, upd_ref, out_ref):
        out_ref[...] = jnp.zeros_like(out_ref)

        def body(group, carry):
            base = group * GROUP
            targets = [rows_ref[base + u] for u in range(GROUP)]
            sums = [
                out_ref[pl.ds(targets[u], 1), :] + upd_ref[pl.ds(base + u, 1), :]
                for u in range(GROUP)
            ]
            for u in range(GROUP):
                out_ref[pl.ds(targets[u], 1), :] = sums[u]
            return carry

        lax.fori_loop(0, count // GROUP, body, 0)

    return pl.pallas_call(
        kernel,
        out_shape=jax.ShapeDtypeStruct((order, columns), jnp.float32),
        grid_spec=pltpu.PrefetchScalarGridSpec(
            num_scalar_prefetch=1,
            grid=(1,),
            in_specs=[pl.BlockSpec((count, columns), lambda i, r: (0, 0))],
            out_specs=pl.BlockSpec((order, columns), lambda i, r: (0, 0)),
        ),
    )(rows, updates)


def gather_rows(rows, table):
    count = rows.shape[0]
    order, columns = table.shape

    def kernel(rows_ref, table_ref, out_ref):
        def body(group, carry):
            base = group * GROUP
            picked = [table_ref[pl.ds(rows_ref[base + u], 1), :] for u in range(GROUP)]
            for u in range(GROUP):
                out_ref[pl.ds(base + u, 1), :] = picked[u]
            return carry

        lax.fori_loop(0, count // GROUP, body, 0)

    return pl.pallas_call(
        kernel,
        out_shape=jax.ShapeDtypeStruct((count, columns), jnp.float32),
        grid_spec=pltpu.PrefetchScalarGridSpec(
            num_scalar_prefetch=1,
            grid=(1,),
            in_specs=[pl.BlockSpec((order, columns), lambda i, r: (0, 0))],
            out_specs=pl.BlockSpec((count, columns), lambda i, r: (0, 0)),
        ),
    )(rows, table)


def owner_sum(parts):
    core = lax.axis_index("core")
    blocks, width, columns = parts.shape
    pairs = parts.reshape(blocks // 2, 2, 8, width * columns // 8)
    mine = jnp.where(core == 1, pairs[:, 1], pairs[:, 0])
    other = jnp.where(core == 1, pairs[:, 0], pairs[:, 1])
    paired = mine + lax.ppermute(other, "core", [(0, 1), (1, 0)])
    spread = lax.all_to_all(paired, ("y", "z"), 0, 0, tiled=False)
    return spread.sum(0).reshape(width, columns)


def share_all(block, blocks):
    width, columns = block.shape
    flat = block.reshape(1, 8, width * columns // 8)
    copies = jnp.broadcast_to(flat, (blocks, 8, width * columns // 8))
    gathered = lax.all_to_all(copies, LEAF_AXES, 0, 0, tiled=False)
    return gathered.reshape(blocks * width, columns)


def gather_columns(part):
    count = lax.axis_size("rhs")
    place = lax.axis_index("rhs")
    shifted = [part] + [
        lax.ppermute(part, "rhs", [(i, (i + step) % count) for i in range(count)])
        for step in range(1, count)
    ]
    ahead = jnp.stack([shifted[(count - t) % count] for t in range(count)])
    ordered = jnp.roll(ahead, place, axis=0)
    rows, width = part.shape
    return ordered.transpose(1, 0, 2).reshape(rows, count * width)


def on_device(
    leaf_rhs, root_rhs, leaf_inverse, leaf_offdiagonal_block, update_rows, leaf_sizes, root_inverse
):
    largest_entry = lax.Precision.HIGH
    leaf_count = leaf_inverse.shape[0]
    leaf_width = leaf_inverse.shape[1]
    touched = leaf_offdiagonal_block.shape[1]
    columns = leaf_rhs.shape[0]
    slot_index = lax.broadcasted_iota(jnp.int32, (leaf_count, leaf_width), 1)
    live_mask = (slot_index < leaf_sizes[:, None]).astype(jnp.float32)
    masked = leaf_inverse * live_mask[:, :, None] * live_mask[:, None, :]
    leaf_forward_sweep = jnp.einsum("clt,lst->cls", leaf_rhs, masked, precision=largest_entry)
    update_terms = jnp.einsum(
        "dwu,wqu->wqd", leaf_forward_sweep, leaf_offdiagonal_block, precision=largest_entry
    )
    root_full = gather_columns(root_inverse)
    root_order = root_full.shape[1]
    width = root_rhs.shape[1]
    blocks = root_order // width
    flat_rows = update_rows.reshape(-1)
    assert touched % GROUP == 0
    accumulated_sum = scatter_rows(
        flat_rows, update_terms.reshape(leaf_count * touched, columns), root_order
    )
    shares = owner_sum(accumulated_sum.reshape(blocks, width, columns))
    reduced = root_rhs.T - shares
    forward_root = jnp.einsum(
        "jc,ij->ic",
        share_all(reduced, blocks),
        root_full,
        precision=largest_entry,
    )
    back_terms = jnp.einsum("ic,ij->jc", forward_root, root_full, precision=largest_entry)
    root_solution = owner_sum(back_terms.reshape(blocks, width, columns))
    root_values = share_all(root_solution, blocks)
    selected_rows = gather_rows(flat_rows, root_values).reshape(leaf_count, touched, columns)
    adjusted_values = leaf_forward_sweep - jnp.einsum(
        "nvr,nvb->rnb", selected_rows, leaf_offdiagonal_block, precision=largest_entry
    )
    leaf_solution = jnp.einsum("cls,lst->clt", adjusted_values, masked, precision=largest_entry)
    return (leaf_solution, root_solution.T)


def solution(mesh):
    sn_size = mesh.shape["sn"]
    fine = Mesh(
        mesh.devices.reshape(sn_size // 16, 8, 2, mesh.shape["rhs"]), ("y", "z", "core", "rhs")
    )
    sn = LEAF_AXES
    in_specs = (
        P("rhs", sn, None),
        P("rhs", sn),
        P(sn, None, None),
        P(sn, None, None),
        P(sn, None),
        P(sn),
        P(sn, "rhs"),
    )
    out_specs = (P("rhs", sn, None), P("rhs", sn))
    return jax.shard_map(
        on_device, mesh=fine, in_specs=in_specs, out_specs=out_specs, check_vma=False
    )
```

```python
import jax
import jax.numpy as jnp
from jax import lax
from jax.experimental import pallas as pl
from jax.experimental.pallas import tpu as pltpu
from jax.sharding import Mesh
from jax.sharding import PartitionSpec as P

LEAF_AXES = ("y", "z", "core")


GROUP = 32


def scatter_rows(rows, updates, order):
    count, columns = updates.shape

    def kernel(rows_ref, upd_ref, out_ref):
        out_ref[...] = jnp.zeros_like(out_ref)

        def body(group, carry):
            base = group * GROUP
            targets = [rows_ref[base + u] for u in range(GROUP)]
            sums = [
                out_ref[pl.ds(targets[u], 1), :] + upd_ref[pl.ds(base + u, 1), :]
                for u in range(GROUP)
            ]
            for u in range(GROUP):
                out_ref[pl.ds(targets[u], 1), :] = sums[u]
            return carry

        lax.fori_loop(0, count // GROUP, body, 0)

    return pl.pallas_call(
        kernel,
        out_shape=jax.ShapeDtypeStruct((order, columns), jnp.float32),
        grid_spec=pltpu.PrefetchScalarGridSpec(
            num_scalar_prefetch=1,
            grid=(1,),
            in_specs=[pl.BlockSpec((count, columns), lambda i, r: (0, 0))],
            out_specs=pl.BlockSpec((order, columns), lambda i, r: (0, 0)),
        ),
    )(rows, updates)


def gather_rows(rows, table):
    count = rows.shape[0]
    order, columns = table.shape

    def kernel(rows_ref, table_ref, out_ref):
        def body(group, carry):
            base = group * GROUP
            picked = [table_ref[pl.ds(rows_ref[base + u], 1), :] for u in range(GROUP)]
            for u in range(GROUP):
                out_ref[pl.ds(base + u, 1), :] = picked[u]
            return carry

        lax.fori_loop(0, count // GROUP, body, 0)

    return pl.pallas_call(
        kernel,
        out_shape=jax.ShapeDtypeStruct((count, columns), jnp.float32),
        grid_spec=pltpu.PrefetchScalarGridSpec(
            num_scalar_prefetch=1,
            grid=(1,),
            in_specs=[pl.BlockSpec((order, columns), lambda i, r: (0, 0))],
            out_specs=pl.BlockSpec((count, columns), lambda i, r: (0, 0)),
        ),
    )(rows, table)


def owner_sum(parts):
    core = lax.axis_index("core")
    blocks, width, columns = parts.shape
    pairs = parts.reshape(blocks // 2, 2, 8, width * columns // 8)
    mine = jnp.where(core == 1, pairs[:, 1], pairs[:, 0])
    other = jnp.where(core == 1, pairs[:, 0], pairs[:, 1])
    paired = mine + lax.ppermute(other, "core", [(0, 1), (1, 0)])
    spread = lax.all_to_all(paired, ("y", "z"), 0, 0, tiled=False)
    return spread.sum(0).reshape(width, columns)


def share_all(block, blocks):
    width, columns = block.shape
    flat = block.reshape(1, 8, width * columns // 8)
    copies = jnp.broadcast_to(flat, (blocks, 8, width * columns // 8))
    gathered = lax.all_to_all(copies, LEAF_AXES, 0, 0, tiled=False)
    return gathered.reshape(blocks * width, columns)


def gather_columns(part):
    count = lax.axis_size("rhs")
    place = lax.axis_index("rhs")
    shifted = [part] + [
        lax.ppermute(part, "rhs", [(i, (i + step) % count) for i in range(count)])
        for step in range(1, count)
    ]
    ahead = jnp.stack([shifted[(count - t) % count] for t in range(count)])
    ordered = jnp.roll(ahead, place, axis=0)
    rows, width = part.shape
    return ordered.transpose(1, 0, 2).reshape(rows, count * width)


def on_device(
    leaf_rhs, root_rhs, leaf_inverse, leaf_offdiagonal_block, update_rows, leaf_sizes, root_inverse
):
    largest_entry = lax.Precision.HIGH
    leaf_count = leaf_inverse.shape[0]
    leaf_width = leaf_inverse.shape[1]
    touched = leaf_offdiagonal_block.shape[1]
    columns = leaf_rhs.shape[0]
    slot_index = lax.broadcasted_iota(jnp.int32, (leaf_count, leaf_width), 1)
    live_mask = (slot_index < leaf_sizes[:, None]).astype(jnp.float32)
    masked = leaf_inverse * live_mask[:, :, None] * live_mask[:, None, :]
    half = leaf_width // 2
    leaf_forward_sweep = jnp.concatenate(
        [
            jnp.einsum(
                "clt,lst->cls", leaf_rhs[:, :, :half], masked[:, :half, :half], precision=largest_entry
            ),
            jnp.einsum("clt,lst->cls", leaf_rhs, masked[:, half:, :], precision=largest_entry),
        ],
        axis=2,
    )
    update_terms = jnp.einsum(
        "dwu,wqu->wqd", leaf_forward_sweep, leaf_offdiagonal_block, precision=largest_entry
    )
    root_full = gather_columns(root_inverse)
    root_order = root_full.shape[1]
    width = root_rhs.shape[1]
    blocks = root_order // width
    flat_rows = update_rows.reshape(-1)
    assert touched % GROUP == 0
    accumulated_sum = scatter_rows(
        flat_rows, update_terms.reshape(leaf_count * touched, columns), root_order
    )
    shares = owner_sum(accumulated_sum.reshape(blocks, width, columns))
    reduced = root_rhs.T - shares
    forward_root = jnp.einsum(
        "jc,ij->ic",
        share_all(reduced, blocks),
        root_full,
        precision=largest_entry,
    )
    back_terms = jnp.einsum("ic,ij->jc", forward_root, root_full, precision=largest_entry)
    root_solution = owner_sum(back_terms.reshape(blocks, width, columns))
    root_values = share_all(root_solution, blocks)
    selected_rows = gather_rows(flat_rows, root_values).reshape(leaf_count, touched, columns)
    adjusted_values = leaf_forward_sweep - jnp.einsum(
        "nvr,nvb->rnb", selected_rows, leaf_offdiagonal_block, precision=largest_entry
    )
    leaf_solution = jnp.concatenate(
        [
            jnp.einsum("cls,lst->clt", adjusted_values, masked[:, :, :half], precision=largest_entry),
            jnp.einsum(
                "cls,lst->clt",
                adjusted_values[:, :, half:],
                masked[:, half:, half:],
                precision=largest_entry,
            ),
        ],
        axis=2,
    )
    return (leaf_solution, root_solution.T)


def solution(mesh):
    sn_size = mesh.shape["sn"]
    fine = Mesh(
        mesh.devices.reshape(sn_size // 16, 8, 2, mesh.shape["rhs"]), ("y", "z", "core", "rhs")
    )
    sn = LEAF_AXES
    in_specs = (
        P("rhs", sn, None),
        P("rhs", sn),
        P(sn, None, None),
        P(sn, None, None),
        P(sn, None),
        P(sn),
        P(sn, "rhs"),
    )
    out_specs = (P("rhs", sn, None), P("rhs", sn))
    return jax.shard_map(
        on_device, mesh=fine, in_specs=in_specs, out_specs=out_specs, check_vma=False
    )
```

```python
import jax
import jax.numpy as jnp
from jax import lax
from jax.experimental import pallas as pl
from jax.experimental.pallas import tpu as pltpu
from jax.sharding import Mesh
from jax.sharding import PartitionSpec as P

LEAF_AXES = ("y", "z", "core")


GROUP = 32


def scatter_rows(rows, updates, order):
    leaves, columns, touched = updates.shape

    def kernel(rows_ref, upd_ref, out_ref, rows_scratch):
        out_ref[...] = jnp.zeros_like(out_ref)

        def leaf(index, carry):
            rows_scratch[...] = upd_ref[index].T

            def body(group, inner):
                base = group * GROUP
                targets = [rows_ref[index * touched + base + u] for u in range(GROUP)]
                sums = [
                    out_ref[pl.ds(targets[u], 1), :] + rows_scratch[pl.ds(base + u, 1), :]
                    for u in range(GROUP)
                ]
                for u in range(GROUP):
                    out_ref[pl.ds(targets[u], 1), :] = sums[u]
                return inner

            return lax.fori_loop(0, touched // GROUP, body, carry)

        lax.fori_loop(0, leaves, leaf, 0)

    return pl.pallas_call(
        kernel,
        out_shape=jax.ShapeDtypeStruct((order, columns), jnp.float32),
        grid_spec=pltpu.PrefetchScalarGridSpec(
            num_scalar_prefetch=1,
            grid=(1,),
            in_specs=[pl.BlockSpec((leaves, columns, touched), lambda i, r: (0, 0, 0))],
            out_specs=pl.BlockSpec((order, columns), lambda i, r: (0, 0)),
            scratch_shapes=[pltpu.VMEM((touched, columns), jnp.float32)],
        ),
    )(rows, updates)


def gather_rows(rows, table):
    count = rows.shape[0]
    order, columns = table.shape

    def kernel(rows_ref, table_ref, out_ref):
        def body(group, carry):
            base = group * GROUP
            picked = [table_ref[pl.ds(rows_ref[base + u], 1), :] for u in range(GROUP)]
            for u in range(GROUP):
                out_ref[pl.ds(base + u, 1), :] = picked[u]
            return carry

        lax.fori_loop(0, count // GROUP, body, 0)

    return pl.pallas_call(
        kernel,
        out_shape=jax.ShapeDtypeStruct((count, columns), jnp.float32),
        grid_spec=pltpu.PrefetchScalarGridSpec(
            num_scalar_prefetch=1,
            grid=(1,),
            in_specs=[pl.BlockSpec((order, columns), lambda i, r: (0, 0))],
            out_specs=pl.BlockSpec((count, columns), lambda i, r: (0, 0)),
        ),
    )(rows, table)


def owner_sum(parts):
    core = lax.axis_index("core")
    blocks, width, columns = parts.shape
    pairs = parts.reshape(blocks // 2, 2, 8, width * columns // 8)
    mine = jnp.where(core == 1, pairs[:, 1], pairs[:, 0])
    other = jnp.where(core == 1, pairs[:, 0], pairs[:, 1])
    paired = mine + lax.ppermute(other, "core", [(0, 1), (1, 0)])
    spread = lax.all_to_all(paired, ("y", "z"), 0, 0, tiled=False)
    return spread.sum(0).reshape(width, columns)


def share_all(block, blocks):
    width, columns = block.shape
    flat = block.reshape(1, 8, width * columns // 8)
    copies = jnp.broadcast_to(flat, (blocks, 8, width * columns // 8))
    gathered = lax.all_to_all(copies, LEAF_AXES, 0, 0, tiled=False)
    return gathered.reshape(blocks * width, columns)


def gather_columns(part):
    count = lax.axis_size("rhs")
    place = lax.axis_index("rhs")
    shifted = [part] + [
        lax.ppermute(part, "rhs", [(i, (i + step) % count) for i in range(count)])
        for step in range(1, count)
    ]
    ahead = jnp.stack([shifted[(count - t) % count] for t in range(count)])
    ordered = jnp.roll(ahead, place, axis=0)
    rows, width = part.shape
    return ordered.transpose(1, 0, 2).reshape(rows, count * width)


def on_device(
    leaf_rhs, root_rhs, leaf_inverse, leaf_offdiagonal_block, update_rows, leaf_sizes, root_inverse
):
    largest_entry = lax.Precision.HIGH
    leaf_count = leaf_inverse.shape[0]
    leaf_width = leaf_inverse.shape[1]
    touched = leaf_offdiagonal_block.shape[1]
    columns = leaf_rhs.shape[0]
    slot_index = lax.broadcasted_iota(jnp.int32, (leaf_count, leaf_width), 1)
    live_mask = (slot_index < leaf_sizes[:, None]).astype(jnp.float32)
    masked = leaf_inverse * live_mask[:, :, None] * live_mask[:, None, :]
    leaf_forward_sweep = jnp.einsum("clt,lst->cls", leaf_rhs, masked, precision=largest_entry)
    update_terms = jnp.einsum(
        "dwu,wqu->wdq", leaf_forward_sweep, leaf_offdiagonal_block, precision=largest_entry
    )
    root_full = gather_columns(root_inverse)
    root_order = root_full.shape[1]
    width = root_rhs.shape[1]
    blocks = root_order // width
    flat_rows = update_rows.reshape(-1)
    assert touched % GROUP == 0
    accumulated_sum = scatter_rows(flat_rows, update_terms, root_order)
    shares = owner_sum(accumulated_sum.reshape(blocks, width, columns))
    reduced = root_rhs.T - shares
    forward_root = jnp.einsum(
        "jc,ij->ic",
        share_all(reduced, blocks),
        root_full,
        precision=largest_entry,
    )
    back_terms = jnp.einsum("ic,ij->jc", forward_root, root_full, precision=largest_entry)
    root_solution = owner_sum(back_terms.reshape(blocks, width, columns))
    root_values = share_all(root_solution, blocks)
    selected_rows = gather_rows(flat_rows, root_values).reshape(leaf_count, touched, columns)
    adjusted_values = leaf_forward_sweep - jnp.einsum(
        "nvr,nvb->rnb", selected_rows, leaf_offdiagonal_block, precision=largest_entry
    )
    leaf_solution = jnp.einsum("cls,lst->clt", adjusted_values, masked, precision=largest_entry)
    return (leaf_solution, root_solution.T)


def solution(mesh):
    sn_size = mesh.shape["sn"]
    fine = Mesh(
        mesh.devices.reshape(sn_size // 16, 8, 2, mesh.shape["rhs"]), ("y", "z", "core", "rhs")
    )
    sn = LEAF_AXES
    in_specs = (
        P("rhs", sn, None),
        P("rhs", sn),
        P(sn, None, None),
        P(sn, None, None),
        P(sn, None),
        P(sn),
        P(sn, "rhs"),
    )
    out_specs = (P("rhs", sn, None), P("rhs", sn))
    return jax.shard_map(
        on_device, mesh=fine, in_specs=in_specs, out_specs=out_specs, check_vma=False
    )
```
